256 devices in a mesh: band: 8 (over y, x_hi), chan: 32 (over x_lo, z, core).
Axes of the slice: x: 4 (x_hi: 2, x_lo: 2; x = x_hi * 2 + x_lo), y: 4, z: 8, core: 2. Of those that a mesh axis runs over, the one named last changes fastest.
Arguments:
- spectra: bfloat16 [2, 64, 512, 8192], P(None, 'band', None, 'chan'), may hold values from -800 to 800
- valid_mask: int32 [512, 8192], P(None, 'chan'), may hold values 0 or 1
Outputs:
- cross_stack: bfloat16 [4, 2, 64, 8192, 256], P(None, None, 'band', 'chan')
The draws below stay inside these ranges and needn't reach their ends.
All inputs are finite; a program needn't handle non-finite values. No bound on the sum of `valid_mask` on one device may be relied on, other than what follows from the above.
Results may differ from the reference program's by a relative error of at most 0.0053.
Values may be sent and summed in bfloat16 or wider, within the bound.
No kernel may reach another device: no remote copies, remote signals or barrier semaphores. Data moves between devices by JAX's collectives and lax.ppermute only.
A program may use at most 64 MiB of HBM per device.

```python
import math
import jax
import jax.numpy as jnp
from jax import lax

CH = 256
W = 512
ROUNDS = 3
NCH = 8192
NBINS = 64
N_CHAN = 32


def draw_spectra(key, part):
    key_base, key_chan, key_window = jax.random.split(key, 3)
    chan_scale = jnp.exp(jax.random.uniform(key_chan, (NCH,), jnp.float32, 0.0, math.log(10.0)))
    window_scale = jnp.exp(jax.random.uniform(key_window, (W, 1), jnp.float32, 0.0, math.log(10.0)))
    bin_place = jnp.arange(NBINS, dtype=jnp.float32) / max(NBINS - 1, 1)
    amplitude = jnp.sqrt(1.0 + 3.0 * bin_place)
    base_values = jax.random.truncated_normal(key_base, -4.0, 4.0, (2, NBINS, W, NCH), jnp.float32)
    result = base_values * amplitude[None, :, None, None] * window_scale[None, None, :, :] * chan_scale[None, None, None, :]
    return result.astype(jnp.bfloat16)


def place_ends(array, stream_key, smallest, top_value):
    index_at = [jax.random.randint(jax.random.fold_in(stream_key, axis), (), 0, length) for axis, length in enumerate(array.shape)]
    widest = array.shape.index(max(array.shape))
    beside = index_at[:widest] + [(index_at[widest] + 1) % array.shape[widest]] + index_at[widest + 1:]
    return array.at[tuple(index_at)].set(smallest).at[tuple(beside)].set(top_value)


def setup_inputs(seed: int = 0) -> dict:
    splits = jax.random.split(jax.random.key(seed), 3)
    return {
        "spectra": draw_spectra(jax.random.fold_in(splits[2], 71), 0),
        "valid_mask": place_ends((jax.random.randint(splits[1], (W, NCH), 0, 4) < 3).astype(jnp.int32), jax.random.fold_in(splits[1], 1), 0, 1),
    }


eps_energy = 1e-06

def cross_pair(left, right, scale):
    flipped = jnp.stack([right[1], -right[0]])
    real_part = jnp.einsum('pwja,pwjb->jab', left, right, precision=lax.Precision.HIGHEST)
    imag_part = jnp.einsum('pwja,pwjb->jab', left, flipped, precision=lax.Precision.HIGHEST)
    return jnp.stack([real_part, imag_part]) * scale

def reference(spectra, valid_mask):
    values = spectra.astype(jnp.float32)
    energy = lax.optimization_barrier(jnp.sum(values * values, axis=(0, 1)))
    window_gain = valid_mask.astype(jnp.float32) / jnp.sqrt(energy / NBINS + eps_energy)
    whitened = (values * window_gain).astype(jnp.bfloat16)
    scale = 1.0 / math.sqrt(W)
    per_bin = jnp.moveaxis(whitened, 1, 0)

    def one_bin(block):
        own_block = block.astype(jnp.float32).reshape(2, W, N_CHAN, CH)
        results = []
        for lag_index in range(ROUNDS + 1):
            partner = jnp.roll(own_block, lag_index, axis=2)
            results.append(cross_pair(own_block, partner, scale).reshape(2, NCH, CH))
        return jnp.stack(results).astype(jnp.bfloat16)
    stacked = lax.map(one_bin, per_bin)
    return jnp.transpose(stacked, (1, 2, 0, 3, 4))
```

```python
import math

import jax
import jax.numpy as jnp
from jax import lax
from jax.sharding import PartitionSpec as P

ROUNDS = 3


eps_energy = 1e-06


def passed_along(value, axis, steps):
    count = lax.axis_size(axis)
    pairs = [(source, (source + steps) % count) for source in range(count)]
    return lax.ppermute(value, axis, pairs)


def cross_block(own_block, partner, scale):
    flipped = jnp.stack([partner[1], -partner[0]])
    real_part = jnp.einsum("pfwa,pfwb->fab", own_block, partner, preferred_element_type=jnp.float32)
    imag_part = jnp.einsum("pfwa,pfwb->fab", own_block, flipped, preferred_element_type=jnp.float32)
    return (jnp.stack([real_part, imag_part]) * scale).astype(jnp.bfloat16)


def whiten(raw, gain):
    return (raw.astype(jnp.float32) * gain).astype(jnp.bfloat16)


def shards(spectra, valid_mask):
    values = spectra.astype(jnp.float32)
    partial_energy = jnp.sum(values * values, axis=(0, 1))
    total_bins = spectra.shape[1] * lax.axis_size("band")
    scale = 1.0 / math.sqrt(spectra.shape[2])
    raws = [spectra]
    for round_idx in range(ROUNDS):
        raws.append(passed_along(raws[-1], "chan", 1))
    energy = lax.psum(partial_energy, "band")
    window_gain = valid_mask.astype(jnp.float32) / jnp.sqrt(energy / total_bins + eps_energy)
    gains = [window_gain]
    for round_idx in range(ROUNDS):
        gains.append(passed_along(gains[-1], "chan", 1))
    whitened = whiten(spectra, window_gain)
    outputs = [cross_block(whitened, whitened, scale)]
    for round_idx in range(1, ROUNDS + 1):
        partner = whiten(raws[round_idx], gains[round_idx])
        outputs.append(cross_block(whitened, partner, scale))
    return jnp.stack(outputs)


def solution(mesh):
    placed = (P(None, "band", None, "chan"), P(None, "chan"))
    return jax.shard_map(
        shards,
        mesh=mesh,
        in_specs=placed,
        out_specs=P(None, None, "band", "chan", None),
        check_vma=False,
    )
```

```python
import math

import jax
import jax.numpy as jnp
from jax import lax
from jax.sharding import PartitionSpec as P

ROUNDS = 3


eps_energy = 1e-06


def passed_along(value, axis, steps):
    count = lax.axis_size(axis)
    pairs = [(source, (source + steps) % count) for source in range(count)]
    return lax.ppermute(value, axis, pairs)


def butterfly_sum(value, axis):
    count = lax.axis_size(axis)
    index = lax.axis_index(axis)
    flat = value.reshape(-1)
    dists = []
    d = count // 2
    while d >= 1:
        dists.append(d)
        d //= 2
    bits = []
    for d in dists:
        half = flat.shape[0] // 2
        low, high = flat[:half], flat[half:]
        bit = (index // d) % 2
        pairs = [(s, s ^ d) for s in range(count)]
        got = lax.ppermute(jnp.where(bit == 0, high, low), axis, pairs)
        flat = jnp.where(bit == 0, low, high) + got
        bits.append(bit)
    for d, bit in zip(reversed(dists), reversed(bits)):
        pairs = [(s, s ^ d) for s in range(count)]
        got = lax.ppermute(flat, axis, pairs)
        flat = jnp.where(bit == 0, jnp.concatenate([flat, got]), jnp.concatenate([got, flat]))
    return flat.reshape(value.shape)


def cross_block(own_block, partner, scale):
    flipped = jnp.stack([partner[1], -partner[0]])
    real_part = jnp.einsum("pfwa,pfwb->fab", own_block, partner, preferred_element_type=jnp.float32)
    imag_part = jnp.einsum("pfwa,pfwb->fab", own_block, flipped, preferred_element_type=jnp.float32)
    return (jnp.stack([real_part, imag_part]) * scale).astype(jnp.bfloat16)


def whiten(raw, gain):
    return (raw.astype(jnp.float32) * gain).astype(jnp.bfloat16)


def shards(spectra, valid_mask):
    values = spectra.astype(jnp.float32)
    partial_energy = jnp.sum(values * values, axis=(0, 1))
    total_bins = spectra.shape[1] * lax.axis_size("band")
    scale = 1.0 / math.sqrt(spectra.shape[2])
    raw_near = passed_along(spectra, "chan", 1)
    energy = butterfly_sum(partial_energy, "band")
    window_gain = valid_mask.astype(jnp.float32) / jnp.sqrt(energy / total_bins + eps_energy)
    gain_near = passed_along(window_gain, "chan", 1)
    whitened = whiten(spectra, window_gain)
    outputs = [cross_block(whitened, whitened, scale)]
    carried = whiten(raw_near, gain_near)
    outputs.append(cross_block(whitened, carried, scale))
    for round_idx in range(2, ROUNDS + 1):
        carried = passed_along(carried, "chan", 1)
        outputs.append(cross_block(whitened, carried, scale))
    return jnp.stack(outputs)


def solution(mesh):
    placed = (P(None, "band", None, "chan"), P(None, "chan"))
    return jax.shard_map(
        shards,
        mesh=mesh,
        in_specs=placed,
        out_specs=P(None, None, "band", "chan", None),
        check_vma=False,
    )
```

```python
import math

import jax
import jax.numpy as jnp
from jax import lax
from jax.sharding import PartitionSpec as P


eps_energy = 1e-06


def moved(value, axis, offset, only_even=False):
    count = lax.axis_size(axis)
    pairs = [(source, (source + offset) % count) for source in range(count) if not only_even or source % 2 == 0]
    return lax.ppermute(value, axis, pairs)


def butterfly_sum(value, axis):
    count = lax.axis_size(axis)
    index = lax.axis_index(axis)
    flat = value.reshape(-1)
    dists = []
    d = count // 2
    while d >= 1:
        dists.append(d)
        d //= 2
    bits = []
    for d in dists:
        half = flat.shape[0] // 2
        low, high = flat[:half], flat[half:]
        bit = (index // d) % 2
        pairs = [(s, s ^ d) for s in range(count)]
        got = lax.ppermute(jnp.where(bit == 0, high, low), axis, pairs)
        flat = jnp.where(bit == 0, low, high) + got
        bits.append(bit)
    for d, bit in zip(reversed(dists), reversed(bits)):
        pairs = [(s, s ^ d) for s in range(count)]
        got = lax.ppermute(flat, axis, pairs)
        flat = jnp.where(bit == 0, jnp.concatenate([flat, got]), jnp.concatenate([got, flat]))
    return flat.reshape(value.shape)


def cross_block(own_block, partner, scale):
    flipped = jnp.stack([partner[1], -partner[0]])
    real_part = jnp.einsum("pfwa,pfwb->fab", own_block, partner, preferred_element_type=jnp.float32)
    imag_part = jnp.einsum("pfwa,pfwb->fab", own_block, flipped, preferred_element_type=jnp.float32)
    return (jnp.stack([real_part, imag_part]) * scale).astype(jnp.bfloat16)


def whiten(raw, gain):
    return (raw.astype(jnp.float32) * gain).astype(jnp.bfloat16)


def shards(spectra, valid_mask):
    values = spectra.astype(jnp.float32)
    partial_energy = jnp.sum(values * values, axis=(0, 1))
    total_bins = spectra.shape[1] * lax.axis_size("band")
    scale = 1.0 / math.sqrt(spectra.shape[2])
    even = lax.axis_index("chan") % 2 == 0
    raw_near = moved(spectra, "chan", 1)
    raw_ahead = moved(spectra, "chan", -2, only_even=True)
    energy = butterfly_sum(partial_energy, "band")
    window_gain = valid_mask.astype(jnp.float32) / jnp.sqrt(energy / total_bins + eps_energy)
    gain_near = moved(window_gain, "chan", 1)
    gain_ahead = moved(window_gain, "chan", -2, only_even=True)
    whitened = whiten(spectra, window_gain)
    near = whiten(raw_near, gain_near)
    ahead = whiten(raw_ahead, gain_ahead)
    second = moved(near, "chan", 1)
    for_above = cross_block(ahead, near, scale)
    for_above, second = lax.optimization_barrier((for_above, second))
    third = moved(second, "chan", 1, only_even=True)
    from_below = moved(for_above, "chan", 2, only_even=True)
    outputs = [
        cross_block(whitened, whitened, scale),
        cross_block(whitened, near, scale),
        cross_block(whitened, second, scale),
        jnp.where(even, from_below, cross_block(whitened, third, scale)),
    ]
    return jnp.stack(outputs)


def solution(mesh):
    placed = (P(None, "band", None, "chan"), P(None, "chan"))
    return jax.shard_map(
        shards,
        mesh=mesh,
        in_specs=placed,
        out_specs=P(None, None, "band", "chan", None),
        check_vma=False,
    )
```

```python
import math

import jax
import jax.numpy as jnp
from jax import lax
from jax.sharding import PartitionSpec as P


eps_energy = 1e-06


def moved(value, axis, offset, only_even=False):
    count = lax.axis_size(axis)
    pairs = [(source, (source + offset) % count) for source in range(count) if not only_even or source % 2 == 0]
    return lax.ppermute(value, axis, pairs)


def butterfly_sum(value, axis):
    count = lax.axis_size(axis)
    index = lax.axis_index(axis)
    flat = value.reshape(-1)
    dists = []
    d = count // 2
    while d >= 1:
        dists.append(d)
        d //= 2
    bits = []
    for d in dists:
        half = flat.shape[0] // 2
        low, high = flat[:half], flat[half:]
        bit = (index // d) % 2
        pairs = [(s, s ^ d) for s in range(count)]
        got = lax.ppermute(jnp.where(bit == 0, high, low), axis, pairs)
        flat = jnp.where(bit == 0, low, high) + got
        bits.append(bit)
    for d, bit in zip(reversed(dists), reversed(bits)):
        pairs = [(s, s ^ d) for s in range(count)]
        got = lax.ppermute(flat, axis, pairs)
        flat = jnp.where(bit == 0, jnp.concatenate([flat, got]), jnp.concatenate([got, flat]))
    return flat.reshape(value.shape)


def cross_block(own_block, partner, scale):
    flipped = jnp.stack([partner[1], -partner[0]])
    real_part = jnp.einsum("pfwa,pfwb->fab", own_block, partner, preferred_element_type=jnp.float32)
    imag_part = jnp.einsum("pfwa,pfwb->fab", own_block, flipped, preferred_element_type=jnp.float32)
    return (jnp.stack([real_part, imag_part]) * scale).astype(jnp.bfloat16)


def whiten(raw, gain):
    return (raw.astype(jnp.float32) * gain).astype(jnp.bfloat16)


def shards(spectra, valid_mask):
    values = spectra.astype(jnp.float32)
    partial_energy = jnp.sum(values * values, axis=(0, 1))
    total_bins = spectra.shape[1] * lax.axis_size("band")
    scale = 1.0 / math.sqrt(spectra.shape[2])
    even = lax.axis_index("chan") % 2 == 0
    raw_near = moved(spectra, "chan", 1)
    raw_ahead = moved(spectra, "chan", -2, only_even=True)
    raw_second = moved(raw_near, "chan", 1)
    energy = butterfly_sum(partial_energy, "band")
    window_gain = valid_mask.astype(jnp.float32) / jnp.sqrt(energy / total_bins + eps_energy)
    gain_near = moved(window_gain, "chan", 1)
    gain_ahead = moved(window_gain, "chan", -2, only_even=True)
    gain_second = moved(gain_near, "chan", 1)
    whitened = whiten(spectra, window_gain)
    near = whiten(raw_near, gain_near)
    ahead = whiten(raw_ahead, gain_ahead)
    for_above = cross_block(ahead, near, scale)
    for_above, raw_second = lax.optimization_barrier((for_above, raw_second))
    second = whiten(raw_second, gain_second)
    third = moved(second, "chan", 1, only_even=True)
    from_below = moved(for_above, "chan", 2, only_even=True)
    outputs = [
        cross_block(whitened, whitened, scale),
        cross_block(whitened, near, scale),
        cross_block(whitened, second, scale),
        jnp.where(even, from_below, cross_block(whitened, third, scale)),
    ]
    return jnp.stack(outputs)


def solution(mesh):
    placed = (P(None, "band", None, "chan"), P(None, "chan"))
    return jax.shard_map(
        shards,
        mesh=mesh,
        in_specs=placed,
        out_specs=P(None, None, "band", "chan", None),
        check_vma=False,
    )
```

```python
import math

import jax
import jax.numpy as jnp
from jax import lax
from jax.sharding import PartitionSpec as P


eps_energy = 1e-06


def moved(value, axis, offset, only_even=False):
    count = lax.axis_size(axis)
    pairs = [(source, (source + offset) % count) for source in range(count) if not only_even or source % 2 == 0]
    return lax.ppermute(value, axis, pairs)


def band_sum(value, axis):
    count = lax.axis_size(axis)
    index = lax.axis_index(axis)
    flat = value.reshape(-1)
    dists = []
    d = count // 2
    while d >= 2:
        dists.append(d)
        d //= 2
    bits = []
    for d in dists:
        half = flat.shape[0] // 2
        low, high = flat[:half], flat[half:]
        bit = (index // d) % 2
        pairs = [(s, s ^ d) for s in range(count)]
        got = lax.ppermute(jnp.where(bit == 0, high, low), axis, pairs)
        flat = jnp.where(bit == 0, low, high) + got
        bits.append(bit)
    for d, bit in zip(reversed(dists), reversed(bits)):
        pairs = [(s, s ^ d) for s in range(count)]
        got = lax.ppermute(flat, axis, pairs)
        flat = jnp.where(bit == 0, jnp.concatenate([flat, got]), jnp.concatenate([got, flat]))
    return flat.reshape(value.shape)


def cross_block(own_block, partner, scale):
    flipped = jnp.stack([partner[1], -partner[0]])
    real_part = jnp.einsum("pfwa,pfwb->fab", own_block, partner, preferred_element_type=jnp.float32)
    imag_part = jnp.einsum("pfwa,pfwb->fab", own_block, flipped, preferred_element_type=jnp.float32)
    return (jnp.stack([real_part, imag_part]) * scale).astype(jnp.bfloat16)


def whiten(raw, gain):
    return (raw.astype(jnp.float32) * gain).astype(jnp.bfloat16)


def shards(spectra, valid_mask):
    values = spectra.astype(jnp.float32)
    partial_energy = jnp.sum(values * values, axis=(0, 1))
    total_bins = spectra.shape[1] * lax.axis_size("band")
    scale = 1.0 / math.sqrt(spectra.shape[2])
    even = lax.axis_index("chan") % 2 == 0
    partial_energy = partial_energy + lax.ppermute(partial_energy, "band", [(s, s ^ 1) for s in range(lax.axis_size("band"))])
    spectra, partial_energy = lax.optimization_barrier((spectra, partial_energy))
    raw_near = moved(spectra, "chan", 1)
    raw_ahead = moved(spectra, "chan", -2, only_even=True)
    energy = band_sum(partial_energy, "band")
    window_gain = valid_mask.astype(jnp.float32) / jnp.sqrt(energy / total_bins + eps_energy)
    gain_near = moved(window_gain, "chan", 1)
    gain_ahead = moved(window_gain, "chan", -2, only_even=True)
    whitened = whiten(spectra, window_gain)
    near = whiten(raw_near, gain_near)
    ahead = whiten(raw_ahead, gain_ahead)
    second = moved(near, "chan", 1)
    for_above = cross_block(ahead, near, scale)
    for_above, second = lax.optimization_barrier((for_above, second))
    third = moved(second, "chan", 1, only_even=True)
    from_below = moved(for_above, "chan", 2, only_even=True)
    outputs = [
        cross_block(whitened, whitened, scale),
        cross_block(whitened, near, scale),
        cross_block(whitened, second, scale),
        jnp.where(even, from_below, cross_block(whitened, third, scale)),
    ]
    return jnp.stack(outputs)


def solution(mesh):
    placed = (P(None, "band", None, "chan"), P(None, "chan"))
    return jax.shard_map(
        shards,
        mesh=mesh,
        in_specs=placed,
        out_specs=P(None, None, "band", "chan", None),
        check_vma=False,
    )
```

```python
import math

import jax
import jax.numpy as jnp
from jax import lax
from jax.sharding import PartitionSpec as P


eps_energy = 1e-06


def moved(value, axis, offset, only_even=False):
    count = lax.axis_size(axis)
    pairs = [(source, (source + offset) % count) for source in range(count) if not only_even or source % 2 == 0]
    return lax.ppermute(value, axis, pairs)


def band_sum(value, axis):
    count = lax.axis_size(axis)
    index = lax.axis_index(axis)
    flat = value.reshape(-1)
    dists = []
    d = count // 2
    while d >= 2:
        dists.append(d)
        d //= 2
    bits = []
    for d in dists:
        half = flat.shape[0] // 2
        low, high = flat[:half], flat[half:]
        bit = (index // d) % 2
        pairs = [(s, s ^ d) for s in range(count)]
        got = lax.ppermute(jnp.where(bit == 0, high, low), axis, pairs)
        flat = jnp.where(bit == 0, low, high) + got
        bits.append(bit)
    for d, bit in zip(reversed(dists), reversed(bits)):
        pairs = [(s, s ^ d) for s in range(count)]
        got = lax.ppermute(flat, axis, pairs)
        flat = jnp.where(bit == 0, jnp.concatenate([flat, got]), jnp.concatenate([got, flat]))
    return flat.reshape(value.shape)


def cross_block(own_block, partner, scale):
    flipped = jnp.stack([partner[1], -partner[0]])
    real_part = jnp.einsum("pfwa,pfwb->fab", own_block, partner, preferred_element_type=jnp.float32)
    imag_part = jnp.einsum("pfwa,pfwb->fab", own_block, flipped, preferred_element_type=jnp.float32)
    return (jnp.stack([real_part, imag_part]) * scale).astype(jnp.bfloat16)


def whiten(raw, gain):
    return (raw.astype(jnp.float32) * gain).astype(jnp.bfloat16)


def shards(spectra, valid_mask):
    values = spectra.astype(jnp.float32)
    partial_energy = jnp.sum(values * values, axis=(0, 1))
    total_bins = spectra.shape[1] * lax.axis_size("band")
    scale = 1.0 / math.sqrt(spectra.shape[2])
    even = lax.axis_index("chan") % 2 == 0
    partial_energy = partial_energy + lax.ppermute(partial_energy, "band", [(s, s ^ 1) for s in range(lax.axis_size("band"))])
    spectra, partial_energy = lax.optimization_barrier((spectra, partial_energy))
    flat_spectra = spectra.reshape(-1, spectra.shape[-1])
    raw_near = moved(flat_spectra, "chan", 1).reshape(spectra.shape)
    raw_ahead = moved(flat_spectra, "chan", -2, only_even=True).reshape(spectra.shape)
    energy = band_sum(partial_energy, "band")
    window_gain = valid_mask.astype(jnp.float32) / jnp.sqrt(energy / total_bins + eps_energy)
    gain_near = moved(window_gain, "chan", 1)
    gain_ahead = moved(window_gain, "chan", -2, only_even=True)
    whitened = whiten(spectra, window_gain)
    near = whiten(raw_near, gain_near)
    ahead = whiten(raw_ahead, gain_ahead)
    second = moved(near, "chan", 1)
    for_above = cross_block(ahead, near, scale)
    own_lag = cross_block(whitened, whitened, scale)
    near_lag = cross_block(whitened, near, scale)
    for_above, second, own_lag, near_lag = lax.optimization_barrier((for_above, second, own_lag, near_lag))
    third = moved(second, "chan", 1, only_even=True)
    from_below = moved(for_above, "chan", 2, only_even=True)
    outputs = [
        own_lag,
        near_lag,
        cross_block(whitened, second, scale),
        jnp.where(even, from_below, cross_block(whitened, third, scale)),
    ]
    return jnp.stack(outputs)


def solution(mesh):
    placed = (P(None, "band", None, "chan"), P(None, "chan"))
    return jax.shard_map(
        shards,
        mesh=mesh,
        in_specs=placed,
        out_specs=P(None, None, "band", "chan", None),
        check_vma=False,
    )
```

```python
import math

import jax
import jax.numpy as jnp
from jax import lax
from jax.sharding import PartitionSpec as P


eps_energy = 1e-06


def moved(value, axis, offset, only_even=False):
    count = lax.axis_size(axis)
    pairs = [(source, (source + offset) % count) for source in range(count) if not only_even or source % 2 == 0]
    return lax.ppermute(value, axis, pairs)


def band_sum(value, axis):
    count = lax.axis_size(axis)
    index = lax.axis_index(axis)
    flat = value.reshape(-1)
    dists = []
    d = count // 2
    while d >= 2:
        dists.append(d)
        d //= 2
    bits = []
    for d in dists:
        half = flat.shape[0] // 2
        low, high = flat[:half], flat[half:]
        bit = (index // d) % 2
        pairs = [(s, s ^ d) for s in range(count)]
        got = lax.ppermute(jnp.where(bit == 0, high, low), axis, pairs)
        flat = jnp.where(bit == 0, low, high) + got
        bits.append(bit)
    for d, bit in zip(reversed(dists), reversed(bits)):
        pairs = [(s, s ^ d) for s in range(count)]
        got = lax.ppermute(flat, axis, pairs)
        flat = jnp.where(bit == 0, jnp.concatenate([flat, got]), jnp.concatenate([got, flat]))
    return flat.reshape(value.shape)


def cross_block(own_block, partner, scale):
    flipped = jnp.stack([partner[1], -partner[0]])
    real_part = jnp.einsum("pfwa,pfwb->fab", own_block, partner, preferred_element_type=jnp.float32)
    imag_part = jnp.einsum("pfwa,pfwb->fab", own_block, flipped, preferred_element_type=jnp.float32)
    return (jnp.stack([real_part, imag_part]) * scale).astype(jnp.bfloat16)


def whiten(raw, gain):
    return (raw.astype(jnp.float32) * gain).astype(jnp.bfloat16)


def shards(spectra, valid_mask):
    values = spectra.astype(jnp.float32)
    partial_energy = jnp.sum(values * values, axis=(0, 1))
    total_bins = spectra.shape[1] * lax.axis_size("band")
    scale = 1.0 / math.sqrt(spectra.shape[2])
    even = lax.axis_index("chan") % 2 == 0
    partial_energy = partial_energy + lax.ppermute(partial_energy, "band", [(s, s ^ 1) for s in range(lax.axis_size("band"))])
    spectra, partial_energy = lax.optimization_barrier((spectra, partial_energy))
    flat_spectra = spectra.reshape(-1, spectra.shape[-1])
    raw_near = moved(flat_spectra, "chan", 1).reshape(spectra.shape)
    raw_ahead = moved(flat_spectra, "chan", -2, only_even=True).reshape(spectra.shape)
    energy = band_sum(partial_energy, "band")
    window_gain = valid_mask.astype(jnp.float32) / jnp.sqrt(energy / total_bins + eps_energy)
    gain_near = moved(window_gain, "chan", 1)
    gain_ahead = moved(window_gain, "chan", -2, only_even=True)
    whitened = whiten(spectra, window_gain)
    near = whiten(raw_near, gain_near)
    ahead = whiten(raw_ahead, gain_ahead)
    for_above = cross_block(ahead, near, scale)
    from_below = moved(for_above, "chan", 2, only_even=True)
    near_sent, from_below = lax.optimization_barrier((near, from_below))
    second = moved(near_sent, "chan", 1)
    third = moved(second, "chan", 1, only_even=True)
    own_lag = cross_block(whitened, whitened, scale)
    near_lag = cross_block(whitened, near, scale)
    outputs = [
        own_lag,
        near_lag,
        cross_block(whitened, second, scale),
        jnp.where(even, from_below, cross_block(whitened, third, scale)),
    ]
    return jnp.stack(outputs)


def solution(mesh):
    placed = (P(None, "band", None, "chan"), P(None, "chan"))
    return jax.shard_map(
        shards,
        mesh=mesh,
        in_specs=placed,
        out_specs=P(None, None, "band", "chan", None),
        check_vma=False,
    )
```

```python
import math

import jax
import jax.numpy as jnp
from jax import lax
from jax.sharding import PartitionSpec as P


eps_energy = 1e-06


def moved(value, axis, offset, only_even=False):
    count = lax.axis_size(axis)
    pairs = [(source, (source + offset) % count) for source in range(count) if not only_even or source % 2 == 0]
    return lax.ppermute(value, axis, pairs)


def band_sum(value, axis):
    count = lax.axis_size(axis)
    index = lax.axis_index(axis)
    flat = value.reshape(-1)
    dists = []
    d = count // 2
    while d >= 2:
        dists.append(d)
        d //= 2
    bits = []
    for d in dists:
        half = flat.shape[0] // 2
        low, high = flat[:half], flat[half:]
        bit = (index // d) % 2
        pairs = [(s, s ^ d) for s in range(count)]
        got = lax.ppermute(jnp.where(bit == 0, high, low), axis, pairs)
        flat = jnp.where(bit == 0, low, high) + got
        bits.append(bit)
    for d, bit in zip(reversed(dists), reversed(bits)):
        pairs = [(s, s ^ d) for s in range(count)]
        got = lax.ppermute(flat, axis, pairs)
        flat = jnp.where(bit == 0, jnp.concatenate([flat, got]), jnp.concatenate([got, flat]))
    return flat.reshape(value.shape)


def cross_block(own_block, partner, scale):
    flipped = jnp.stack([partner[1], -partner[0]])
    real_part = jnp.einsum("pfwa,pfwb->fab", own_block, partner, preferred_element_type=jnp.float32)
    imag_part = jnp.einsum("pfwa,pfwb->fab", own_block, flipped, preferred_element_type=jnp.float32)
    return (jnp.stack([real_part, imag_part]) * scale).astype(jnp.bfloat16)


def whiten(raw, gain):
    return (raw.astype(jnp.float32) * gain).astype(jnp.bfloat16)


def shards(spectra, valid_mask):
    values = spectra.astype(jnp.float32)
    partial_energy = jnp.sum(values * values, axis=(0, 1))
    total_bins = spectra.shape[1] * lax.axis_size("band")
    scale = 1.0 / math.sqrt(spectra.shape[2])
    even = lax.axis_index("chan") % 2 == 0
    partial_energy = partial_energy + lax.ppermute(partial_energy, "band", [(s, s ^ 1) for s in range(lax.axis_size("band"))])
    spectra, partial_energy = lax.optimization_barrier((spectra, partial_energy))
    flat_spectra = spectra.reshape(-1, spectra.shape[-1])
    raw_near = moved(flat_spectra, "chan", 1).reshape(spectra.shape)
    raw_ahead = moved(flat_spectra, "chan", -2, only_even=True).reshape(spectra.shape)
    energy = band_sum(partial_energy, "band")
    window_gain = valid_mask.astype(jnp.float32) / jnp.sqrt(energy / total_bins + eps_energy)
    gain_near = moved(window_gain, "chan", 1)
    gain_ahead = moved(window_gain, "chan", -2, only_even=True)
    whitened = whiten(spectra, window_gain)
    near = whiten(raw_near, gain_near)
    ahead = whiten(raw_ahead, gain_ahead)
    second = moved(near, "chan", 1)
    for_above = cross_block(ahead, near, scale)
    own_lag = cross_block(whitened, whitened, scale)
    near_lag = cross_block(whitened, near, scale)
    for_above, second, own_lag, near_lag = lax.optimization_barrier((for_above, second, own_lag, near_lag))
    third = moved(second, "chan", 1, only_even=True)
    from_below = moved(for_above, "chan", 2, only_even=True)
    lag_two = cross_block(whitened, second, scale)
    lag_three = cross_block(whitened, third, scale)
    early = jnp.stack([own_lag, near_lag, lag_two, lag_three])
    early, second = lax.optimization_barrier((early, second))
    last = jnp.where(even, from_below, early[3])
    return lax.dynamic_update_slice_in_dim(early, last[None], 3, axis=0)


def solution(mesh):
    placed = (P(None, "band", None, "chan"), P(None, "chan"))
    return jax.shard_map(
        shards,
        mesh=mesh,
        in_specs=placed,
        out_specs=P(None, None, "band", "chan", None),
        check_vma=False,
    )
```

```python
import math

import jax
import jax.numpy as jnp
from jax import lax
from jax.sharding import PartitionSpec as P


eps_energy = 1e-06


def moved(value, axis, offset, only_even=False, only_odd=False):
    count = lax.axis_size(axis)
    pairs = [(source, (source + offset) % count) for source in range(count)
             if not (only_even and source % 2) and not (only_odd and source % 2 == 0)]
    return lax.ppermute(value, axis, pairs)


def band_sum(value, axis):
    count = lax.axis_size(axis)
    index = lax.axis_index(axis)
    flat = value.reshape(-1)
    dists = []
    d = count // 2
    while d >= 2:
        dists.append(d)
        d //= 2
    bits = []
    for d in dists:
        half = flat.shape[0] // 2
        low, high = flat[:half], flat[half:]
        bit = (index // d) % 2
        pairs = [(s, s ^ d) for s in range(count)]
        got = lax.ppermute(jnp.where(bit == 0, high, low), axis, pairs)
        flat = jnp.where(bit == 0, low, high) + got
        bits.append(bit)
    for d, bit in zip(reversed(dists), reversed(bits)):
        pairs = [(s, s ^ d) for s in range(count)]
        got = lax.ppermute(flat, axis, pairs)
        flat = jnp.where(bit == 0, jnp.concatenate([flat, got]), jnp.concatenate([got, flat]))
    return flat.reshape(value.shape)


def cross_block(own_block, partner, scale):
    flipped = jnp.stack([partner[1], -partner[0]])
    real_part = jnp.einsum("pfwa,pfwb->fab", own_block, partner, preferred_element_type=jnp.float32)
    imag_part = jnp.einsum("pfwa,pfwb->fab", own_block, flipped, preferred_element_type=jnp.float32)
    return (jnp.stack([real_part, imag_part]) * scale).astype(jnp.bfloat16)


def whiten(raw, gain):
    return (raw.astype(jnp.float32) * gain).astype(jnp.bfloat16)


def shards(spectra, valid_mask):
    values = spectra.astype(jnp.float32)
    partial_energy = jnp.sum(values * values, axis=(0, 1))
    total_bins = spectra.shape[1] * lax.axis_size("band")
    scale = 1.0 / math.sqrt(spectra.shape[2])
    even = lax.axis_index("chan") % 2 == 0
    partial_energy = partial_energy + lax.ppermute(partial_energy, "band", [(s, s ^ 1) for s in range(lax.axis_size("band"))])
    spectra, partial_energy = lax.optimization_barrier((spectra, partial_energy))
    flat_spectra = spectra.reshape(-1, spectra.shape[-1])
    raw_near = moved(flat_spectra, "chan", 1).reshape(spectra.shape)
    raw_ahead = moved(flat_spectra, "chan", -2, only_even=True).reshape(spectra.shape)
    raw_mate = moved(flat_spectra, "chan", -1, only_odd=True).reshape(spectra.shape)
    energy = band_sum(partial_energy, "band")
    window_gain = valid_mask.astype(jnp.float32) / jnp.sqrt(energy / total_bins + eps_energy)
    gain_near = moved(window_gain, "chan", 1)
    gain_ahead = moved(window_gain, "chan", -2, only_even=True)
    gain_mate = moved(window_gain, "chan", -1, only_odd=True)
    whitened = whiten(spectra, window_gain)
    near = whiten(raw_near, gain_near)
    ahead = whiten(raw_ahead, gain_ahead)
    second = moved(near, "chan", 1)
    for_above = cross_block(ahead, near, scale)
    own_lag = cross_block(whitened, whitened, scale)
    near_lag = cross_block(whitened, near, scale)
    for_above, second, own_lag, near_lag = lax.optimization_barrier((for_above, second, own_lag, near_lag))
    from_below = moved(for_above, "chan", 2, only_even=True)
    mate = whiten(raw_mate, gain_mate)
    for_mate = cross_block(mate, second, scale)
    from_mate = moved(for_mate, "chan", 1, only_even=True)
    lag_two = cross_block(whitened, second, scale)
    early = jnp.stack([own_lag, near_lag, lag_two, jnp.zeros_like(own_lag)])
    early, second = lax.optimization_barrier((early, second))
    last = jnp.where(even, from_below, from_mate)
    return lax.dynamic_update_slice_in_dim(early, last[None], 3, axis=0)


def solution(mesh):
    placed = (P(None, "band", None, "chan"), P(None, "chan"))
    return jax.shard_map(
        shards,
        mesh=mesh,
        in_specs=placed,
        out_specs=P(None, None, "band", "chan", None),
        check_vma=False,
    )
```

```python
import math

import jax
import jax.numpy as jnp
from jax import lax
from jax.sharding import PartitionSpec as P


eps_energy = 1e-06


def moved(value, axis, offset, only_even=False, only_odd=False):
    count = lax.axis_size(axis)
    pairs = [(source, (source + offset) % count) for source in range(count)
             if not (only_even and source % 2) and not (only_odd and source % 2 == 0)]
    return lax.ppermute(value, axis, pairs)


def band_sum(value, axis):
    count = lax.axis_size(axis)
    index = lax.axis_index(axis)
    flat = value.reshape(-1)
    dists = []
    d = count // 2
    while d >= 2:
        dists.append(d)
        d //= 2
    bits = []
    for d in dists:
        half = flat.shape[0] // 2
        low, high = flat[:half], flat[half:]
        bit = (index // d) % 2
        pairs = [(s, s ^ d) for s in range(count)]
        got = lax.ppermute(jnp.where(bit == 0, high, low), axis, pairs)
        flat = jnp.where(bit == 0, low, high) + got
        bits.append(bit)
    flat = flat + lax.ppermute(flat, axis, [(s, s ^ 1) for s in range(count)])
    for d, bit in zip(reversed(dists), reversed(bits)):
        pairs = [(s, s ^ d) for s in range(count)]
        got = lax.ppermute(flat, axis, pairs)
        flat = jnp.where(bit == 0, jnp.concatenate([flat, got]), jnp.concatenate([got, flat]))
    return flat.reshape(value.shape)


def cross_block(own_block, partner, scale):
    flipped = jnp.stack([partner[1], -partner[0]])
    real_part = jnp.einsum("pfwa,pfwb->fab", own_block, partner, preferred_element_type=jnp.float32)
    imag_part = jnp.einsum("pfwa,pfwb->fab", own_block, flipped, preferred_element_type=jnp.float32)
    return (jnp.stack([real_part, imag_part]) * scale).astype(jnp.bfloat16)


def whiten(raw, gain):
    return (raw.astype(jnp.float32) * gain).astype(jnp.bfloat16)


def shards(spectra, valid_mask):
    values = spectra.astype(jnp.float32)
    partial_energy = jnp.sum(values * values, axis=(0, 1))
    total_bins = spectra.shape[1] * lax.axis_size("band")
    scale = 1.0 / math.sqrt(spectra.shape[2])
    even = lax.axis_index("chan") % 2 == 0
    flat_spectra = spectra.reshape(-1, spectra.shape[-1])
    raw_near = moved(flat_spectra, "chan", 1).reshape(spectra.shape)
    raw_ahead = moved(flat_spectra, "chan", -2, only_even=True).reshape(spectra.shape)
    raw_mate = moved(flat_spectra, "chan", -1, only_odd=True).reshape(spectra.shape)
    energy = band_sum(partial_energy, "band")
    window_gain = valid_mask.astype(jnp.float32) / jnp.sqrt(energy / total_bins + eps_energy)
    gain_near = moved(window_gain, "chan", 1)
    gain_ahead = moved(window_gain, "chan", -2, only_even=True)
    gain_mate = moved(window_gain, "chan", -1, only_odd=True)
    whitened = whiten(spectra, window_gain)
    near = whiten(raw_near, gain_near)
    ahead = whiten(raw_ahead, gain_ahead)
    second = moved(near, "chan", 1)
    for_above = cross_block(ahead, near, scale)
    own_lag = cross_block(whitened, whitened, scale)
    near_lag = cross_block(whitened, near, scale)
    for_above, second, own_lag, near_lag = lax.optimization_barrier((for_above, second, own_lag, near_lag))
    from_below = moved(for_above, "chan", 2, only_even=True)
    mate = whiten(raw_mate, gain_mate)
    for_mate = cross_block(mate, second, scale)
    from_mate = moved(for_mate, "chan", 1, only_even=True)
    lag_two = cross_block(whitened, second, scale)
    early = jnp.stack([own_lag, near_lag, lag_two, jnp.zeros_like(own_lag)])
    early, second = lax.optimization_barrier((early, second))
    last = jnp.where(even, from_below, from_mate)
    return lax.dynamic_update_slice_in_dim(early, last[None], 3, axis=0)


def solution(mesh):
    placed = (P(None, "band", None, "chan"), P(None, "chan"))
    return jax.shard_map(
        shards,
        mesh=mesh,
        in_specs=placed,
        out_specs=P(None, None, "band", "chan", None),
        check_vma=False,
    )
```

```python
import math

import jax
import jax.numpy as jnp
from jax import lax
from jax.sharding import PartitionSpec as P


eps_energy = 1e-06


def moved(value, axis, offset, only_even=False, only_odd=False):
    count = lax.axis_size(axis)
    pairs = [(source, (source + offset) % count) for source in range(count)
             if not (only_even and source % 2) and not (only_odd and source % 2 == 0)]
    return lax.ppermute(value, axis, pairs)


def band_sum(value, axis):
    count = lax.axis_size(axis)
    index = lax.axis_index(axis)
    flat = value.reshape(-1)
    dists = []
    d = count // 2
    while d >= 2:
        dists.append(d)
        d //= 2
    bits = []
    for d in dists:
        half = flat.shape[0] // 2
        low, high = flat[:half], flat[half:]
        bit = (index // d) % 2
        pairs = [(s, s ^ d) for s in range(count)]
        got = lax.ppermute(jnp.where(bit == 0, high, low), axis, pairs)
        flat = jnp.where(bit == 0, low, high) + got
        bits.append(bit)
    for d, bit in zip(reversed(dists), reversed(bits)):
        pairs = [(s, s ^ d) for s in range(count)]
        got = lax.ppermute(flat, axis, pairs)
        flat = jnp.where(bit == 0, jnp.concatenate([flat, got]), jnp.concatenate([got, flat]))
    return flat.reshape(value.shape)


def cross_block(own_block, partner, scale):
    flipped = jnp.stack([partner[1], -partner[0]])
    real_part = jnp.einsum("pfwa,pfwb->fab", own_block, partner, preferred_element_type=jnp.float32)
    imag_part = jnp.einsum("pfwa,pfwb->fab", own_block, flipped, preferred_element_type=jnp.float32)
    return (jnp.stack([real_part, imag_part]) * scale).astype(jnp.bfloat16)


def whiten(raw, gain):
    return (raw.astype(jnp.float32) * gain).astype(jnp.bfloat16)


def shards(spectra, valid_mask):
    values = spectra.astype(jnp.float32)
    partial_energy = jnp.sum(values * values, axis=(0, 1))
    total_bins = spectra.shape[1] * lax.axis_size("band")
    scale = 1.0 / math.sqrt(spectra.shape[2])
    even = lax.axis_index("chan") % 2 == 0
    partial_energy = partial_energy + lax.ppermute(partial_energy, "band", [(s, s ^ 1) for s in range(lax.axis_size("band"))])
    spectra, partial_energy = lax.optimization_barrier((spectra, partial_energy))
    flat_spectra = spectra.reshape(-1, spectra.shape[-1])
    raw_near = moved(flat_spectra, "chan", 1).reshape(spectra.shape)
    raw_ahead = moved(flat_spectra, "chan", -2, only_even=True).reshape(spectra.shape)
    raw_odd_ahead = moved(flat_spectra, "chan", -3, only_odd=True).reshape(spectra.shape)
    energy = band_sum(partial_energy, "band")
    window_gain = valid_mask.astype(jnp.float32) / jnp.sqrt(energy / total_bins + eps_energy)
    gain_near = moved(window_gain, "chan", 1)
    gain_ahead = moved(window_gain, "chan", -2, only_even=True)
    gain_odd_ahead = moved(window_gain, "chan", -3, only_odd=True)
    whitened = whiten(spectra, window_gain)
    near = whiten(raw_near, gain_near)
    ahead = whiten(raw_ahead, gain_ahead)
    odd_ahead = whiten(raw_odd_ahead, gain_odd_ahead)
    lag2_above = moved(cross_block(ahead, whitened, scale), "chan", 2, only_even=True)
    lag3_above = moved(cross_block(ahead, near, scale), "chan", 2, only_even=True)
    lag3_mate = moved(cross_block(odd_ahead, whitened, scale), "chan", 3, only_even=True)
    second = moved(near, "chan", 1, only_even=True)
    outputs = [
        cross_block(whitened, whitened, scale),
        cross_block(whitened, near, scale),
        jnp.where(even, lag2_above, cross_block(whitened, second, scale)),
        jnp.where(even, lag3_above, lag3_mate),
    ]
    return jnp.stack(outputs)


def solution(mesh):
    placed = (P(None, "band", None, "chan"), P(None, "chan"))
    return jax.shard_map(
        shards,
        mesh=mesh,
        in_specs=placed,
        out_specs=P(None, None, "band", "chan", None),
        check_vma=False,
    )
```

```python
import math

import jax
import jax.numpy as jnp
from jax import lax
from jax.sharding import PartitionSpec as P


eps_energy = 1e-06


def moved(value, axis, offset, only_even=False, only_odd=False):
    count = lax.axis_size(axis)
    pairs = [(source, (source + offset) % count) for source in range(count)
             if not (only_even and source % 2) and not (only_odd and source % 2 == 0)]
    return lax.ppermute(value, axis, pairs)


def band_sum(value, axis):
    count = lax.axis_size(axis)
    index = lax.axis_index(axis)
    flat = value.reshape(-1)
    dists = []
    d = count // 2
    while d >= 2:
        dists.append(d)
        d //= 2
    bits = []
    for d in dists:
        half = flat.shape[0] // 2
        low, high = flat[:half], flat[half:]
        bit = (index // d) % 2
        pairs = [(s, s ^ d) for s in range(count)]
        got = lax.ppermute(jnp.where(bit == 0, high, low), axis, pairs)
        flat = jnp.where(bit == 0, low, high) + got
        bits.append(bit)
    for d, bit in zip(reversed(dists), reversed(bits)):
        pairs = [(s, s ^ d) for s in range(count)]
        got = lax.ppermute(flat, axis, pairs)
        flat = jnp.where(bit == 0, jnp.concatenate([flat, got]), jnp.concatenate([got, flat]))
    return flat.reshape(value.shape)


def cross_block(own_block, partner, scale):
    flipped = jnp.stack([partner[1], -partner[0]])
    real_part = jnp.einsum("pfwa,pfwb->fab", own_block, partner, preferred_element_type=jnp.float32)
    imag_part = jnp.einsum("pfwa,pfwb->fab", own_block, flipped, preferred_element_type=jnp.float32)
    return (jnp.stack([real_part, imag_part]) * scale).astype(jnp.bfloat16)


def whiten(raw, gain):
    return (raw.astype(jnp.float32) * gain).astype(jnp.bfloat16)


def shards(spectra, valid_mask):
    values = spectra.astype(jnp.float32)
    partial_energy = jnp.sum(values * values, axis=(0, 1))
    total_bins = spectra.shape[1] * lax.axis_size("band")
    scale = 1.0 / math.sqrt(spectra.shape[2])
    even = lax.axis_index("chan") % 2 == 0
    partial_energy = partial_energy + lax.ppermute(partial_energy, "band", [(s, s ^ 1) for s in range(lax.axis_size("band"))])
    spectra, partial_energy = lax.optimization_barrier((spectra, partial_energy))
    flat_spectra = spectra.reshape(-1, spectra.shape[-1])
    raw_near = moved(flat_spectra, "chan", 1).reshape(spectra.shape)
    raw_ahead = moved(flat_spectra, "chan", -2, only_even=True).reshape(spectra.shape)
    raw_odd_ahead = moved(flat_spectra, "chan", -3, only_odd=True).reshape(spectra.shape)
    energy = band_sum(partial_energy, "band")
    window_gain = valid_mask.astype(jnp.float32) / jnp.sqrt(energy / total_bins + eps_energy)
    gain_near = moved(window_gain, "chan", 1)
    gain_ahead = moved(window_gain, "chan", -2, only_even=True)
    gain_odd_ahead = moved(window_gain, "chan", -3, only_odd=True)
    whitened = whiten(spectra, window_gain)
    near = whiten(raw_near, gain_near)
    ahead = whiten(raw_ahead, gain_ahead)
    raw_odd_ahead, gain_near = lax.optimization_barrier((raw_odd_ahead, gain_near))
    odd_ahead = whiten(raw_odd_ahead, gain_odd_ahead)
    lag2_above = moved(cross_block(ahead, whitened, scale), "chan", 2, only_even=True)
    lag3_above = moved(cross_block(ahead, near, scale), "chan", 2, only_even=True)
    lag3_mate = moved(cross_block(odd_ahead, whitened, scale), "chan", 3, only_even=True)
    second = moved(near, "chan", 1, only_even=True)
    outputs = [
        cross_block(whitened, whitened, scale),
        cross_block(whitened, near, scale),
        jnp.where(even, lag2_above, cross_block(whitened, second, scale)),
        jnp.where(even, lag3_above, lag3_mate),
    ]
    return jnp.stack(outputs)


def solution(mesh):
    placed = (P(None, "band", None, "chan"), P(None, "chan"))
    return jax.shard_map(
        shards,
        mesh=mesh,
        in_specs=placed,
        out_specs=P(None, None, "band", "chan", None),
        check_vma=False,
    )
```

```python
import math

import jax
import jax.numpy as jnp
from jax import lax
from jax.sharding import PartitionSpec as P


eps_energy = 1e-06


def moved(value, axis, offset, only_even=False, only_odd=False):
    count = lax.axis_size(axis)
    pairs = [(source, (source + offset) % count) for source in range(count)
             if not (only_even and source % 2) and not (only_odd and source % 2 == 0)]
    return lax.ppermute(value, axis, pairs)


def band_sum(value, axis):
    count = lax.axis_size(axis)
    index = lax.axis_index(axis)
    flat = value.reshape(-1)
    dists = []
    d = count // 2
    while d >= 2:
        dists.append(d)
        d //= 2
    bits = []
    for d in dists:
        half = flat.shape[0] // 2
        low, high = flat[:half], flat[half:]
        bit = (index // d) % 2
        pairs = [(s, s ^ d) for s in range(count)]
        got = lax.ppermute(jnp.where(bit == 0, high, low), axis, pairs)
        flat = jnp.where(bit == 0, low, high) + got
        bits.append(bit)
    for d, bit in zip(reversed(dists), reversed(bits)):
        pairs = [(s, s ^ d) for s in range(count)]
        got = lax.ppermute(flat, axis, pairs)
        flat = jnp.where(bit == 0, jnp.concatenate([flat, got]), jnp.concatenate([got, flat]))
    return flat.reshape(value.shape)


def cross_block(own_block, partner, scale):
    flipped = jnp.stack([partner[1], -partner[0]])
    real_part = jnp.einsum("pfwa,pfwb->fab", own_block, partner, preferred_element_type=jnp.float32)
    imag_part = jnp.einsum("pfwa,pfwb->fab", own_block, flipped, preferred_element_type=jnp.float32)
    return (jnp.stack([real_part, imag_part]) * scale).astype(jnp.bfloat16)


def whiten(raw, gain):
    return (raw.astype(jnp.float32) * gain).astype(jnp.bfloat16)


def shards(spectra, valid_mask):
    values = spectra.astype(jnp.float32)
    partial_energy = jnp.sum(values * values, axis=(0, 1))
    total_bins = spectra.shape[1] * lax.axis_size("band")
    scale = 1.0 / math.sqrt(spectra.shape[2])
    even = lax.axis_index("chan") % 2 == 0
    partial_energy = partial_energy + lax.ppermute(partial_energy, "band", [(s, s ^ 1) for s in range(lax.axis_size("band"))])
    spectra, partial_energy = lax.optimization_barrier((spectra, partial_energy))
    flat_spectra = spectra.reshape(-1, spectra.shape[-1])
    raw_near = moved(flat_spectra, "chan", 1).reshape(spectra.shape)
    raw_ahead = moved(flat_spectra, "chan", -2, only_even=True).reshape(spectra.shape)
    raw_mate = moved(flat_spectra, "chan", -1, only_odd=True).reshape(spectra.shape)
    energy = band_sum(partial_energy, "band")
    window_gain = valid_mask.astype(jnp.float32) / jnp.sqrt(energy / total_bins + eps_energy)
    gain_near = moved(window_gain.astype(jnp.bfloat16), "chan", 1).astype(jnp.float32)
    gain_ahead = moved(window_gain, "chan", -2, only_even=True)
    gain_mate = moved(window_gain, "chan", -1, only_odd=True)
    whitened = whiten(spectra, window_gain)
    near = whiten(raw_near, gain_near)
    ahead = whiten(raw_ahead, gain_ahead)
    second = moved(near, "chan", 1)
    for_above = cross_block(ahead, near, scale)
    own_lag = cross_block(whitened, whitened, scale)
    near_lag = cross_block(whitened, near, scale)
    for_above, second, own_lag, near_lag = lax.optimization_barrier((for_above, second, own_lag, near_lag))
    from_below = moved(for_above, "chan", 2, only_even=True)
    mate = whiten(raw_mate, gain_mate)
    for_mate = cross_block(mate, second, scale)
    from_mate = moved(for_mate, "chan", 1, only_even=True)
    lag_two = cross_block(whitened, second, scale)
    early = jnp.stack([own_lag, near_lag, lag_two, jnp.zeros_like(own_lag)])
    early, second = lax.optimization_barrier((early, second))
    last = jnp.where(even, from_below, from_mate)
    return lax.dynamic_update_slice_in_dim(early, last[None], 3, axis=0)


def solution(mesh):
    placed = (P(None, "band", None, "chan"), P(None, "chan"))
    return jax.shard_map(
        shards,
        mesh=mesh,
        in_specs=placed,
        out_specs=P(None, None, "band", "chan", None),
        check_vma=False,
    )
```

```python
import math

import jax
import jax.numpy as jnp
from jax import lax
from jax.sharding import PartitionSpec as P


eps_energy = 1e-06


def moved(value, axis, offset, only_even=False, only_odd=False):
    count = lax.axis_size(axis)
    pairs = [(source, (source + offset) % count) for source in range(count)
             if not (only_even and source % 2) and not (only_odd and source % 2 == 0)]
    return lax.ppermute(value, axis, pairs)


def band_sum(value, axis):
    count = lax.axis_size(axis)
    index = lax.axis_index(axis)
    flat = value.reshape(-1)
    dists = []
    d = count // 2
    while d >= 2:
        dists.append(d)
        d //= 2
    bits = []
    for d in dists:
        half = flat.shape[0] // 2
        low, high = flat[:half], flat[half:]
        bit = (index // d) % 2
        pairs = [(s, s ^ d) for s in range(count)]
        got = lax.ppermute(jnp.where(bit == 0, high, low), axis, pairs)
        flat = jnp.where(bit == 0, low, high) + got
        bits.append(bit)
    for d, bit in zip(reversed(dists), reversed(bits)):
        pairs = [(s, s ^ d) for s in range(count)]
        got = lax.ppermute(flat, axis, pairs)
        flat = jnp.where(bit == 0, jnp.concatenate([flat, got]), jnp.concatenate([got, flat]))
    return flat.reshape(value.shape)


def cross_block(own_block, partner, scale):
    flipped = jnp.stack([partner[1], -partner[0]])
    real_part = jnp.einsum("pfwa,pfwb->fab", own_block, partner, preferred_element_type=jnp.float32)
    imag_part = jnp.einsum("pfwa,pfwb->fab", own_block, flipped, preferred_element_type=jnp.float32)
    return (jnp.stack([real_part, imag_part]) * scale).astype(jnp.bfloat16)


def whiten(raw, gain):
    return (raw.astype(jnp.float32) * gain).astype(jnp.bfloat16)


def shards(spectra, valid_mask):
    values = spectra.astype(jnp.float32)
    band_pairs = [(s, s ^ 1) for s in range(lax.axis_size("band"))]
    window_half = spectra.shape[2] // 2
    halves = []
    for part in (values[:, :, :window_half], values[:, :, window_half:]):
        partial = jnp.sum(part * part, axis=(0, 1))
        halves.append(partial + lax.ppermute(partial, "band", band_pairs))
    partial_energy = jnp.concatenate(halves, axis=0)
    total_bins = spectra.shape[1] * lax.axis_size("band")
    scale = 1.0 / math.sqrt(spectra.shape[2])
    even = lax.axis_index("chan") % 2 == 0
    spectra, partial_energy = lax.optimization_barrier((spectra, partial_energy))
    flat_spectra = spectra.reshape(-1, spectra.shape[-1])
    raw_near = moved(flat_spectra, "chan", 1).reshape(spectra.shape)
    raw_ahead = moved(flat_spectra, "chan", -2, only_even=True).reshape(spectra.shape)
    raw_mate = moved(flat_spectra, "chan", -1, only_odd=True).reshape(spectra.shape)
    energy = band_sum(partial_energy, "band")
    window_gain = valid_mask.astype(jnp.float32) / jnp.sqrt(energy / total_bins + eps_energy)
    gain_near = moved(window_gain.astype(jnp.bfloat16), "chan", 1).astype(jnp.float32)
    gain_ahead = moved(window_gain, "chan", -2, only_even=True)
    gain_mate = moved(window_gain, "chan", -1, only_odd=True)
    whitened = whiten(spectra, window_gain)
    near = whiten(raw_near, gain_near)
    ahead = whiten(raw_ahead, gain_ahead)
    second = moved(near, "chan", 1)
    for_above = cross_block(ahead, near, scale)
    own_lag = cross_block(whitened, whitened, scale)
    near_lag = cross_block(whitened, near, scale)
    for_above, second, own_lag, near_lag = lax.optimization_barrier((for_above, second, own_lag, near_lag))
    from_below = moved(for_above, "chan", 2, only_even=True)
    mate = whiten(raw_mate, gain_mate)
    for_mate = cross_block(mate, second, scale)
    from_mate = moved(for_mate, "chan", 1, only_even=True)
    lag_two = cross_block(whitened, second, scale)
    early = jnp.stack([own_lag, near_lag, lag_two, jnp.zeros_like(own_lag)])
    early, second = lax.optimization_barrier((early, second))
    last = jnp.where(even, from_below, from_mate)
    return lax.dynamic_update_slice_in_dim(early, last[None], 3, axis=0)


def solution(mesh):
    placed = (P(None, "band", None, "chan"), P(None, "chan"))
    return jax.shard_map(
        shards,
        mesh=mesh,
        in_specs=placed,
        out_specs=P(None, None, "band", "chan", None),
        check_vma=False,
    )
```

```python
import math

import jax
import jax.numpy as jnp
from jax import lax
from jax.sharding import PartitionSpec as P


eps_energy = 1e-06


def moved(value, axis, offset, only_even=False, only_odd=False):
    count = lax.axis_size(axis)
    pairs = [(source, (source + offset) % count) for source in range(count)
             if not (only_even and source % 2) and not (only_odd and source % 2 == 0)]
    return lax.ppermute(value, axis, pairs)


def band_sum(value, axis):
    count = lax.axis_size(axis)
    index = lax.axis_index(axis)
    flat = value.reshape(-1)
    dists = []
    d = count // 2
    while d >= 2:
        dists.append(d)
        d //= 2
    bits = []
    for d in dists:
        half = flat.shape[0] // 2
        low, high = flat[:half], flat[half:]
        bit = (index // d) % 2
        pairs = [(s, s ^ d) for s in range(count)]
        got = lax.ppermute(jnp.where(bit == 0, high, low), axis, pairs)
        flat = jnp.where(bit == 0, low, high) + got
        bits.append(bit)
    for d, bit in zip(reversed(dists), reversed(bits)):
        pairs = [(s, s ^ d) for s in range(count)]
        got = lax.ppermute(flat, axis, pairs)
        flat = jnp.where(bit == 0, jnp.concatenate([flat, got]), jnp.concatenate([got, flat]))
    return flat.reshape(value.shape)


def cross_block(own_block, partner, scale):
    flipped = jnp.stack([partner[1], -partner[0]])
    real_part = jnp.einsum("pfwa,pfwb->fab", own_block, partner, preferred_element_type=jnp.float32)
    imag_part = jnp.einsum("pfwa,pfwb->fab", own_block, flipped, preferred_element_type=jnp.float32)
    return (jnp.stack([real_part, imag_part]) * scale).astype(jnp.bfloat16)


def whiten(raw, gain):
    return (raw.astype(jnp.float32) * gain).astype(jnp.bfloat16)


def shards(spectra, valid_mask):
    values = spectra.astype(jnp.float32)
    partial_energy = jnp.sum(values * values, axis=(0, 1))
    total_bins = spectra.shape[1] * lax.axis_size("band")
    scale = 1.0 / math.sqrt(spectra.shape[2])
    even = lax.axis_index("chan") % 2 == 0
    partial_energy = partial_energy + lax.ppermute(partial_energy, "band", [(s, s ^ 1) for s in range(lax.axis_size("band"))])
    spectra, partial_energy = lax.optimization_barrier((spectra, partial_energy))
    flat_spectra = spectra.reshape(-1, spectra.shape[-1])
    raw_near = moved(flat_spectra, "chan", 1).reshape(spectra.shape)
    raw_ahead = moved(flat_spectra, "chan", -2, only_even=True).reshape(spectra.shape)
    raw_mate = moved(flat_spectra, "chan", -1, only_odd=True).reshape(spectra.shape)
    energy = band_sum(partial_energy, "band")
    window_gain = valid_mask.astype(jnp.float32) / jnp.sqrt(energy / total_bins + eps_energy)
    gain_near = moved(window_gain.astype(jnp.bfloat16), "chan", 1).astype(jnp.float32)
    gain_ahead = moved(window_gain, "chan", -2, only_even=True)
    gain_mate = moved(window_gain, "chan", -1, only_odd=True)
    whitened = whiten(spectra, window_gain)
    near_parts = [whiten(raw_near[k], gain_near) for k in range(raw_near.shape[0])]
    near = jnp.stack(near_parts)
    ahead = whiten(raw_ahead, gain_ahead)
    second_parts = tuple(moved(x, "chan", 1) for x in near_parts)
    for_above = cross_block(ahead, near, scale)
    own_lag = cross_block(whitened, whitened, scale)
    near_lag = cross_block(whitened, near, scale)
    for_above, second_parts, own_lag, near_lag = lax.optimization_barrier((for_above, second_parts, own_lag, near_lag))
    second = jnp.stack(second_parts)
    from_below = moved(for_above, "chan", 2, only_even=True)
    mate = whiten(raw_mate, gain_mate)
    for_mate = cross_block(mate, second, scale)
    from_mate = moved(for_mate, "chan", 1, only_even=True)
    lag_two = cross_block(whitened, second, scale)
    early = jnp.stack([own_lag, near_lag, lag_two, jnp.zeros_like(own_lag)])
    early, _ = lax.optimization_barrier((early, second_parts[0]))
    last = jnp.where(even, from_below, from_mate)
    return lax.dynamic_update_slice_in_dim(early, last[None], 3, axis=0)


def solution(mesh):
    placed = (P(None, "band", None, "chan"), P(None, "chan"))
    return jax.shard_map(
        shards,
        mesh=mesh,
        in_specs=placed,
        out_specs=P(None, None, "band", "chan", None),
        check_vma=False,
    )
```

```python
import math

import jax
import jax.numpy as jnp
from jax import lax
from jax.sharding import PartitionSpec as P


eps_energy = 1e-06


def moved(value, axis, offset, only_even=False, only_odd=False):
    count = lax.axis_size(axis)
    pairs = [(source, (source + offset) % count) for source in range(count)
             if not (only_even and source % 2) and not (only_odd and source % 2 == 0)]
    return lax.ppermute(value, axis, pairs)


def band_sum(value, axis):
    count = lax.axis_size(axis)
    index = lax.axis_index(axis)
    flat = value.reshape(-1)
    dists = []
    d = count // 2
    while d >= 2:
        dists.append(d)
        d //= 2
    bits = []
    for d in dists:
        half = flat.shape[0] // 2
        low, high = flat[:half], flat[half:]
        bit = (index // d) % 2
        pairs = [(s, s ^ d) for s in range(count)]
        got = lax.ppermute(jnp.where(bit == 0, high, low), axis, pairs)
        flat = jnp.where(bit == 0, low, high) + got
        bits.append(bit)
    for d, bit in zip(reversed(dists), reversed(bits)):
        pairs = [(s, s ^ d) for s in range(count)]
        got = lax.ppermute(flat, axis, pairs)
        flat = jnp.where(bit == 0, jnp.concatenate([flat, got]), jnp.concatenate([got, flat]))
    return flat.reshape(value.shape)


def cross_block(own_block, partner, scale):
    flipped = jnp.stack([partner[1], -partner[0]])
    real_part = jnp.einsum("pfwa,pfwb->fab", own_block, partner, preferred_element_type=jnp.float32)
    imag_part = jnp.einsum("pfwa,pfwb->fab", own_block, flipped, preferred_element_type=jnp.float32)
    return (jnp.stack([real_part, imag_part]) * scale).astype(jnp.bfloat16)


def whiten(raw, gain):
    return (raw.astype(jnp.float32) * gain).astype(jnp.bfloat16)


def shards(spectra, valid_mask):
    values = spectra.astype(jnp.float32)
    partial_energy = jnp.sum(values * values, axis=(0, 1))
    total_bins = spectra.shape[1] * lax.axis_size("band")
    scale = 1.0 / math.sqrt(spectra.shape[2])
    even = lax.axis_index("chan") % 2 == 0
    partial_energy = partial_energy + lax.ppermute(partial_energy.astype(jnp.bfloat16), "band", [(s, s ^ 1) for s in range(lax.axis_size("band"))]).astype(jnp.float32)
    spectra, partial_energy = lax.optimization_barrier((spectra, partial_energy))
    flat_spectra = spectra.reshape(-1, spectra.shape[-1])
    raw_near = moved(flat_spectra, "chan", 1).reshape(spectra.shape)
    raw_ahead = moved(flat_spectra, "chan", -2, only_even=True).reshape(spectra.shape)
    raw_mate = moved(flat_spectra, "chan", -1, only_odd=True).reshape(spectra.shape)
    energy = band_sum(partial_energy, "band")
    window_gain = valid_mask.astype(jnp.float32) / jnp.sqrt(energy / total_bins + eps_energy)
    gain_near = moved(window_gain.astype(jnp.bfloat16), "chan", 1).astype(jnp.float32)
    gain_ahead = moved(window_gain, "chan", -2, only_even=True)
    gain_mate = moved(window_gain, "chan", -1, only_odd=True)
    whitened = whiten(spectra, window_gain)
    near = whiten(raw_near, gain_near)
    ahead = whiten(raw_ahead, gain_ahead)
    second = moved(near, "chan", 1)
    for_above = cross_block(ahead, near, scale)
    own_lag = cross_block(whitened, whitened, scale)
    near_lag = cross_block(whitened, near, scale)
    for_above, second, own_lag, near_lag = lax.optimization_barrier((for_above, second, own_lag, near_lag))
    from_below = moved(for_above, "chan", 2, only_even=True)
    mate = whiten(raw_mate, gain_mate)
    for_mate = cross_block(mate, second, scale)
    from_mate = moved(for_mate, "chan", 1, only_even=True)
    lag_two = cross_block(whitened, second, scale)
    early = jnp.stack([own_lag, near_lag, lag_two, jnp.zeros_like(own_lag)])
    early, second = lax.optimization_barrier((early, second))
    last = jnp.where(even, from_below, from_mate)
    return lax.dynamic_update_slice_in_dim(early, last[None], 3, axis=0)


def solution(mesh):
    placed = (P(None, "band", None, "chan"), P(None, "chan"))
    return jax.shard_map(
        shards,
        mesh=mesh,
        in_specs=placed,
        out_specs=P(None, None, "band", "chan", None),
        check_vma=False,
    )
```
